128 devices in a mesh: aux: 4 (over x), row: 32 (over z, y, core).
Axes of the slice: x: 4, y: 4, z: 4, core: 2. Of those that a mesh axis runs over, the one named last changes fastest.
Arguments:
- b_tiles: bfloat16 [4, 32768, 2048], P('aux', 'row'), may hold values from -0.125 to 0.125
- occ_coeff: bfloat16 [32768, 256], P('row'), may hold values from -3 to 3
- tile_blocks: int32 [256, 16], P('row'), may hold values from 0 to 255, as said below
- screen_mask: int32 [256, 16], P('row'), may hold values from 0 to 1, as said below
Outputs:
- exchange: bfloat16 [32768, 32, 4, 256], P('row', None, 'aux')
The draws below stay inside these ranges and needn't reach their ends.
Inputs may be any that keep to these rules, and one draw needn't show every extreme that they name: `tile_blocks`: each entry names a basis block at most 8 blocks away from its own row's block; the first slot of every block names the block itself. `screen_mask`: in every basis block the kept slots come first; some block keeps all 16.
All inputs are finite; a program needn't handle non-finite values.
Results may differ from the reference program's by a relative error of at most 0.0057.
Values may be sent and summed in bfloat16 or wider, within the bound.
No kernel may reach another device: no remote copies, remote signals or barrier semaphores. Data moves between devices by JAX's collectives and lax.ppermute only.
A program may use at most 128 MiB of HBM per device.

```python
import jax
import jax.numpy as jnp
from jax import lax

OCC = 256
BS = 128
BLK_DEV = 8
SLOTS = 16
MU_DEV = 1024
NBLK = 256
NBF = 32768
P_TOT = 4
SUB = 256
N_AUX = 4
N_ROW = 32


def draw_tile_blocks(key, part):
    spread_count = 2 * BLK_DEV + 1
    column_index = jnp.arange(spread_count, dtype=jnp.int32)[None, :]
    scores = jax.random.randint(key, (NBLK, spread_count), 0, 2 ** 20) * spread_count + column_index
    scores = jnp.where(column_index == BLK_DEV, -1, scores)
    ranking = jnp.argsort(scores, axis=1, stable=True).astype(jnp.int32)
    offsets = ranking[:, :SLOTS] - BLK_DEV
    anchor = jnp.arange(NBLK, dtype=jnp.int32)[:, None]
    ahead = anchor + offsets
    inside = (ahead >= 0) & (ahead < NBLK)
    return jnp.where(inside, ahead, anchor - offsets).astype(jnp.int32)


def draw_screen_mask(key, part):
    devices = NBLK // BLK_DEV
    key_heavy, key_force, key_high, key_low = jax.random.split(jax.random.fold_in(key, 7), 4)
    heavy = jax.random.randint(key_heavy, (devices,), 0, 4) == 0
    forced = jax.random.randint(key_force, (), 0, devices)
    heavy = heavy | (jnp.arange(devices, dtype=jnp.int32) == forced)
    owners = jnp.arange(NBLK, dtype=jnp.int32) // BLK_DEV
    high = jax.random.randint(key_high, (NBLK,), 12, SLOTS + 1)
    low = jax.random.randint(key_low, (NBLK,), 2, 7)
    counts = jnp.where(heavy[owners], high, low)
    counts = jnp.where(jnp.arange(NBLK, dtype=jnp.int32) == forced * BLK_DEV, SLOTS, counts)
    return (jnp.arange(SLOTS, dtype=jnp.int32)[None, :] < counts[:, None]).astype(jnp.int32)


def block_levels(rng, dims, cuts, smallest, top_value):
    def one(position, shards_of):
        steps = jax.random.uniform(jax.random.fold_in(jax.random.fold_in(rng, 6), position), (shards_of,), jnp.float32, smallest / len(cuts), top_value / len(cuts))
        return jnp.repeat(jnp.exp(steps), dims[position] // shards_of).reshape((-1,) + (1,) * (len(dims) - position - 1))

    loudness = one(*cuts[0])
    for cut in cuts[1:]:
        loudness = loudness * one(*cut)
    return loudness


def gaussian(own_key, extent, spread, limit, cuts=(), kind=jnp.bfloat16):
    values = spread * jax.random.normal(own_key, extent, jnp.float32)
    if cuts:
        values = values * block_levels(own_key, extent, cuts, -0.22, 0.18)
    return jnp.clip(values, -limit, limit).astype(kind)


def setup_inputs(seed: int = 0) -> dict:
    key_of = jax.random.split(jax.random.key(seed), 5)
    b_tiles = gaussian(key_of[0], (P_TOT, NBF, SLOTS * BS), (SLOTS * BS) ** -0.5, 0.125, ((0, 4), (1, 32)))
    occ_coeff = gaussian(key_of[1], (NBF, OCC), 0.5, 3.0, ((0, 32),))
    tile_blocks = draw_tile_blocks(jax.random.fold_in(key_of[4], 71), 0)
    screen_mask = draw_screen_mask(jax.random.fold_in(key_of[4], 71), 0)
    return {"b_tiles": b_tiles, "occ_coeff": occ_coeff, "tile_blocks": tile_blocks, "screen_mask": screen_mask}


def reference(b_tiles, occ_coeff, tile_blocks, screen_mask):
    coeff_blocks = occ_coeff.reshape(NBLK, BS, OCC).astype(jnp.float32)
    tiles = b_tiles.reshape(P_TOT, NBLK, BS, SLOTS, BS)

    def one_block(index):
        block_tiles = lax.dynamic_index_in_dim(tiles, index, 1, keepdims=False).astype(jnp.float32)
        columns = lax.dynamic_index_in_dim(tile_blocks, index, 0, keepdims=False)
        live = lax.dynamic_index_in_dim(screen_mask, index, 0, keepdims=False).astype(jnp.float32)
        picked = coeff_blocks[columns] * live[:, None, None]
        return jnp.einsum("pmsn,sni->pmi", block_tiles, picked, precision=lax.Precision.HIGHEST)

    halves = lax.map(one_block, jnp.arange(NBLK, dtype=jnp.int32)).astype(jnp.bfloat16)
    slab_all = jnp.transpose(halves, (1, 0, 2, 3)).reshape(P_TOT, NBF, OCC).astype(jnp.float32)

    def one_rows(index):
        rows_now = lax.dynamic_slice_in_dim(slab_all, index * MU_DEV, MU_DEV, 1)
        return jnp.einsum("pmi,pli->ml", rows_now, slab_all, precision=lax.Precision.HIGHEST).astype(jnp.bfloat16)

    matrix = lax.map(one_rows, jnp.arange(N_ROW, dtype=jnp.int32))
    return matrix.reshape(NBF, N_ROW, N_AUX, SUB)
```

```python
import jax
import jax.numpy as jnp
from jax import lax
from jax.sharding import Mesh, PartitionSpec as P


def with_halo(block, sides, width):
    for axis, dim in sides:
        count = lax.axis_size(axis)
        forward = [(i, i + 1) for i in range(count - 1)]
        backward = [(target, source) for source, target in forward]
        low = lax.ppermute(
            lax.slice_in_dim(block, block.shape[dim] - width, None, axis=dim), axis, forward
        )
        high = lax.ppermute(lax.slice_in_dim(block, 0, width, axis=dim), axis, backward)
        block = jnp.concatenate([low, block, high], axis=dim)
    return block


ROW = ("rzy", "core")


def per_device(b_tiles, occ_coeff, tile_blocks, screen_mask):
    p_local, rows_local, stored = b_tiles.shape
    blocks_local, slot_count = tile_blocks.shape
    block_size = rows_local // blocks_local
    orbitals = occ_coeff.shape[1]
    aux_count = lax.axis_size("aux")
    row_index = lax.axis_index(ROW)
    extended = with_halo(occ_coeff, ((ROW, 0),), rows_local)
    coeff_blocks = extended.reshape(3 * blocks_local, block_size, orbitals)
    local_index = tile_blocks - (row_index - 1) * blocks_local
    picked = jnp.take(coeff_blocks, local_index, axis=0)
    keep_mask = screen_mask.astype(jnp.bfloat16)
    tiles_five = b_tiles.reshape(p_local, blocks_local, block_size, slot_count, block_size)
    masked = picked * keep_mask[:, :, None, None]
    half_sum = jnp.einsum(
        "pbmsn,bsni->pbmi", tiles_five, masked, preferred_element_type=jnp.float32
    )
    half_local = half_sum.astype(jnp.bfloat16).reshape(p_local, rows_local, orbitals)
    slab_rows = lax.all_gather(half_local, "aux", axis=0, tiled=True)
    share = rows_local // aux_count
    piece = lax.dynamic_slice_in_dim(slab_rows, lax.axis_index("aux") * share, share, axis=1)
    plane = lax.all_gather(piece, "rzy", axis=0)
    partner = lax.all_gather(plane, "core", axis=1)
    chips, cores = partner.shape[:2]
    partner = partner.reshape(chips * cores, *piece.shape)
    result = jnp.einsum("pmi,rpki->mrk", slab_rows, partner, preferred_element_type=jnp.float32)
    return result.astype(jnp.bfloat16).reshape(rows_local, chips * cores, 1, share)


def solution(mesh):
    aux_count, row_count = mesh.devices.shape
    devices = mesh.devices.reshape(aux_count, row_count // 2, 2)
    split_mesh = Mesh(devices, ("aux",) + ROW)
    in_specs = (P("aux", ROW, None), P(ROW, None), P(ROW, None), P(ROW, None))
    out_specs = P(ROW, None, "aux", None)
    return jax.shard_map(
        per_device, mesh=split_mesh, in_specs=in_specs, out_specs=out_specs, check_vma=False
    )
```

```python
import jax
import jax.numpy as jnp
from jax import lax
from jax.sharding import Mesh, PartitionSpec as P


def with_halo(block, sides, width):
    for axis, dim in sides:
        count = lax.axis_size(axis)
        forward = [(i, i + 1) for i in range(count - 1)]
        backward = [(target, source) for source, target in forward]
        low = lax.ppermute(
            lax.slice_in_dim(block, block.shape[dim] - width, None, axis=dim), axis, forward
        )
        high = lax.ppermute(lax.slice_in_dim(block, 0, width, axis=dim), axis, backward)
        block = jnp.concatenate([low, block, high], axis=dim)
    return block


ROW = ("rzy", "core")


def per_device(b_tiles, occ_coeff, tile_blocks, screen_mask):
    p_local, rows_local, stored = b_tiles.shape
    blocks_local, slot_count = tile_blocks.shape
    block_size = rows_local // blocks_local
    orbitals = occ_coeff.shape[1]
    aux_count = lax.axis_size("aux")
    row_index = lax.axis_index(ROW)
    extended = with_halo(occ_coeff, ((ROW, 0),), rows_local)
    coeff_blocks = extended.reshape(3 * blocks_local, block_size, orbitals)
    local_index = tile_blocks - (row_index - 1) * blocks_local
    picked = jnp.take(coeff_blocks, local_index, axis=0)
    keep_mask = screen_mask.astype(jnp.bfloat16)
    tiles_five = b_tiles.reshape(p_local, blocks_local, block_size, slot_count, block_size)
    masked = picked * keep_mask[:, :, None, None]
    half_sum = jnp.einsum(
        "pbmsn,bsni->pbmi", tiles_five, masked, preferred_element_type=jnp.float32
    )
    half_local = half_sum.astype(jnp.bfloat16).reshape(p_local, rows_local, orbitals)
    aux_index = lax.axis_index("aux")
    shifted = [half_local[0]]
    for shift in range(1, aux_count):
        pairs = [(i, (i + shift) % aux_count) for i in range(aux_count)]
        shifted.append(lax.ppermute(half_local[0], "aux", pairs))
    slab_rows = jnp.stack(shifted)
    share = rows_local // aux_count
    piece = lax.dynamic_slice_in_dim(slab_rows, aux_index * share, share, axis=1)
    partner = lax.all_gather(piece, ROW, axis=0)
    row_count = partner.shape[0]
    result = jnp.einsum("pmi,rpki->mrk", slab_rows, partner, preferred_element_type=jnp.float32)
    return result.astype(jnp.bfloat16).reshape(rows_local, row_count, 1, share)


def solution(mesh):
    aux_count, row_count = mesh.devices.shape
    devices = mesh.devices.reshape(aux_count, row_count // 2, 2)
    split_mesh = Mesh(devices, ("aux",) + ROW)
    in_specs = (P("aux", ROW, None), P(ROW, None), P(ROW, None), P(ROW, None))
    out_specs = P(ROW, None, "aux", None)
    return jax.shard_map(
        per_device, mesh=split_mesh, in_specs=in_specs, out_specs=out_specs, check_vma=False
    )
```

```python
import jax
import jax.numpy as jnp
from jax import lax
from jax.sharding import Mesh, PartitionSpec as P


def with_halo(block, sides, width):
    for axis, dim in sides:
        count = lax.axis_size(axis)
        forward = [(i, i + 1) for i in range(count - 1)]
        backward = [(target, source) for source, target in forward]
        low = lax.ppermute(
            lax.slice_in_dim(block, block.shape[dim] - width, None, axis=dim), axis, forward
        )
        high = lax.ppermute(lax.slice_in_dim(block, 0, width, axis=dim), axis, backward)
        block = jnp.concatenate([low, block, high], axis=dim)
    return block


ROW = ("rzy", "core")


def per_device(b_tiles, occ_coeff, tile_blocks, screen_mask):
    p_local, rows_local, stored = b_tiles.shape
    blocks_local, slot_count = tile_blocks.shape
    block_size = rows_local // blocks_local
    orbitals = occ_coeff.shape[1]
    aux_count = lax.axis_size("aux")
    row_index = lax.axis_index(ROW)
    extended = with_halo(occ_coeff, ((ROW, 0),), rows_local)
    coeff_blocks = extended.reshape(3 * blocks_local, block_size, orbitals)
    local_index = tile_blocks - (row_index - 1) * blocks_local
    picked = jnp.take(coeff_blocks, local_index, axis=0)
    keep_mask = screen_mask.astype(jnp.bfloat16)
    tiles_five = b_tiles.reshape(p_local, blocks_local, block_size, slot_count, block_size)
    masked = picked * keep_mask[:, :, None, None]
    half_sum = jnp.einsum(
        "pbmsn,bsni->pbmi", tiles_five, masked, preferred_element_type=jnp.float32
    )
    half_local = half_sum.astype(jnp.bfloat16).reshape(p_local, rows_local, orbitals)
    aux_index = lax.axis_index("aux")
    share = rows_local // aux_count
    own = half_local[0]
    pieces = [lax.dynamic_slice_in_dim(own, aux_index * share, share, axis=0)]
    shifted = [own]
    for shift in range(1, aux_count):
        pairs = [(i, (i + shift) % aux_count) for i in range(aux_count)]
        target = (aux_index + shift) % aux_count
        outgoing = lax.dynamic_slice_in_dim(own, target * share, share, axis=0)
        pieces.append(lax.ppermute(outgoing, "aux", pairs))
        shifted.append(lax.ppermute(own, "aux", pairs))
    piece = jnp.stack(pieces)
    slab_rows = jnp.stack(shifted)
    chunk_count = 2
    chunk = share // chunk_count
    results = []
    for c in range(chunk_count):
        part = lax.slice_in_dim(piece, c * chunk, (c + 1) * chunk, axis=1)
        partner = lax.all_gather(part, ROW, axis=0)
        results.append(
            jnp.einsum("pmi,rpki->mrk", slab_rows, partner, preferred_element_type=jnp.float32)
            .astype(jnp.bfloat16)
        )
    result = jnp.concatenate(results, axis=2)
    return result.reshape(rows_local, result.shape[1], 1, share)


def solution(mesh):
    aux_count, row_count = mesh.devices.shape
    devices = mesh.devices.reshape(aux_count, row_count // 2, 2)
    split_mesh = Mesh(devices, ("aux",) + ROW)
    in_specs = (P("aux", ROW, None), P(ROW, None), P(ROW, None), P(ROW, None))
    out_specs = P(ROW, None, "aux", None)
    return jax.shard_map(
        per_device, mesh=split_mesh, in_specs=in_specs, out_specs=out_specs, check_vma=False
    )
```

```python
import jax
import jax.numpy as jnp
from jax import lax
from jax.sharding import Mesh, PartitionSpec as P


def with_halo(block, sides, width):
    for axis, dim in sides:
        count = lax.axis_size(axis)
        forward = [(i, i + 1) for i in range(count - 1)]
        backward = [(target, source) for source, target in forward]
        low = lax.ppermute(
            lax.slice_in_dim(block, block.shape[dim] - width, None, axis=dim), axis, forward
        )
        high = lax.ppermute(lax.slice_in_dim(block, 0, width, axis=dim), axis, backward)
        block = jnp.concatenate([low, block, high], axis=dim)
    return block


ROW = ("rzy", "core")


def per_device(b_tiles, occ_coeff, tile_blocks, screen_mask):
    p_local, rows_local, stored = b_tiles.shape
    blocks_local, slot_count = tile_blocks.shape
    block_size = rows_local // blocks_local
    orbitals = occ_coeff.shape[1]
    aux_count = lax.axis_size("aux")
    row_index = lax.axis_index(ROW)
    extended = with_halo(occ_coeff, ((ROW, 0),), rows_local)
    coeff_blocks = extended.reshape(3 * blocks_local, block_size, orbitals)
    local_index = tile_blocks - (row_index - 1) * blocks_local
    picked = jnp.take(coeff_blocks, local_index, axis=0)
    keep_mask = screen_mask.astype(jnp.bfloat16)
    tiles_five = b_tiles.reshape(p_local, blocks_local, block_size, slot_count, block_size)
    masked = picked * keep_mask[:, :, None, None]
    half_sum = jnp.einsum(
        "pbmsn,bsni->pbmi", tiles_five, masked, preferred_element_type=jnp.float32
    )
    half_local = half_sum.astype(jnp.bfloat16).reshape(p_local, rows_local, orbitals)
    aux_index = lax.axis_index("aux")
    share = rows_local // aux_count
    own = half_local[0]
    pieces = [lax.dynamic_slice_in_dim(own, aux_index * share, share, axis=0)]
    shifted = [own]
    for shift in range(1, aux_count):
        pairs = [(i, (i + shift) % aux_count) for i in range(aux_count)]
        target = (aux_index + shift) % aux_count
        outgoing = lax.dynamic_slice_in_dim(own, target * share, share, axis=0)
        pieces.append(lax.ppermute(outgoing, "aux", pairs))
        shifted.append(lax.ppermute(own, "aux", pairs))
    piece = jnp.stack(pieces)
    slab_rows = jnp.stack(shifted)
    partner = lax.all_gather(piece, ROW, axis=0)
    result = jnp.einsum("pmi,rpki->mrk", slab_rows, partner, preferred_element_type=jnp.float32)
    return result.astype(jnp.bfloat16).reshape(rows_local, partner.shape[0], 1, share)


def solution(mesh):
    aux_count, row_count = mesh.devices.shape
    devices = mesh.devices.reshape(aux_count, row_count // 2, 2)
    split_mesh = Mesh(devices, ("aux",) + ROW)
    in_specs = (P("aux", ROW, None), P(ROW, None), P(ROW, None), P(ROW, None))
    out_specs = P(ROW, None, "aux", None)
    return jax.shard_map(
        per_device, mesh=split_mesh, in_specs=in_specs, out_specs=out_specs, check_vma=False
    )
```

```python
import jax
import jax.numpy as jnp
from jax import lax
from jax.experimental import pallas as pl
from jax.experimental.pallas import tpu as pltpu
from jax.sharding import Mesh, PartitionSpec as P


def with_halo(block, sides, width):
    for axis, dim in sides:
        count = lax.axis_size(axis)
        forward = [(i, i + 1) for i in range(count - 1)]
        backward = [(target, source) for source, target in forward]
        low = lax.ppermute(
            lax.slice_in_dim(block, block.shape[dim] - width, None, axis=dim), axis, forward
        )
        high = lax.ppermute(lax.slice_in_dim(block, 0, width, axis=dim), axis, backward)
        block = jnp.concatenate([low, block, high], axis=dim)
    return block


ROW = ("rzy", "core")


def per_device(b_tiles, occ_coeff, tile_blocks, screen_mask):
    p_local, rows_local, stored = b_tiles.shape
    blocks_local, slot_count = tile_blocks.shape
    block_size = rows_local // blocks_local
    orbitals = occ_coeff.shape[1]
    aux_count = lax.axis_size("aux")
    row_index = lax.axis_index(ROW)
    extended = with_halo(occ_coeff, ((ROW, 0),), rows_local)
    coeff_blocks = extended.reshape(3 * blocks_local, block_size, orbitals)
    local_index = tile_blocks - (row_index - 1) * blocks_local
    window = coeff_blocks.shape[0]
    local_index = jnp.clip(local_index, 0, window - 1).astype(jnp.int32)
    tiles = b_tiles.reshape(rows_local, stored)
    extended = extended.reshape(window * block_size, orbitals)

    def kernel(index_ref, mask_ref, tile_ref, coeff_ref, out_ref, acc_ref):
        b = pl.program_id(0)
        acc_ref[...] = jnp.zeros_like(acc_ref)
        for s in range(slot_count):
            @pl.when(mask_ref[b, s] != 0)
            def _():
                start = pl.multiple_of(index_ref[b, s] * block_size, block_size)
                coeff = coeff_ref[pl.ds(start, block_size), :]
                tile = tile_ref[:, s * block_size:(s + 1) * block_size]
                acc_ref[...] += jnp.dot(tile, coeff, preferred_element_type=jnp.float32)
        out_ref[...] = acc_ref[...].astype(out_ref.dtype)

    half_local = pl.pallas_call(
        kernel,
        grid_spec=pltpu.PrefetchScalarGridSpec(
            num_scalar_prefetch=2,
            grid=(blocks_local,),
            in_specs=[
                pl.BlockSpec((block_size, stored), lambda b, li, mk: (b, 0)),
                pl.BlockSpec((window * block_size, orbitals), lambda b, li, mk: (0, 0)),
            ],
            out_specs=pl.BlockSpec((block_size, orbitals), lambda b, li, mk: (b, 0)),
            scratch_shapes=[pltpu.VMEM((block_size, orbitals), jnp.float32)],
        ),
        out_shape=jax.ShapeDtypeStruct((rows_local, orbitals), jnp.bfloat16),
    )(local_index, screen_mask, tiles, extended)
    half_local = half_local.reshape(p_local, rows_local, orbitals)
    aux_index = lax.axis_index("aux")
    share = rows_local // aux_count
    own = half_local[0]
    pieces = [lax.dynamic_slice_in_dim(own, aux_index * share, share, axis=0)]
    shifted = [own]
    for shift in range(1, aux_count):
        pairs = [(i, (i + shift) % aux_count) for i in range(aux_count)]
        target = (aux_index + shift) % aux_count
        outgoing = lax.dynamic_slice_in_dim(own, target * share, share, axis=0)
        pieces.append(lax.ppermute(outgoing, "aux", pairs))
        shifted.append(lax.ppermute(own, "aux", pairs))
    piece = jnp.stack(pieces)
    slab_rows = jnp.stack(shifted)
    partner = lax.all_gather(piece, ROW, axis=0)
    result = jnp.einsum("pmi,rpki->mrk", slab_rows, partner, preferred_element_type=jnp.float32)
    return result.astype(jnp.bfloat16).reshape(rows_local, partner.shape[0], 1, share)


def solution(mesh):
    aux_count, row_count = mesh.devices.shape
    devices = mesh.devices.reshape(aux_count, row_count // 2, 2)
    split_mesh = Mesh(devices, ("aux",) + ROW)
    in_specs = (P("aux", ROW, None), P(ROW, None), P(ROW, None), P(ROW, None))
    out_specs = P(ROW, None, "aux", None)
    return jax.shard_map(
        per_device, mesh=split_mesh, in_specs=in_specs, out_specs=out_specs, check_vma=False
    )
```

```python
import jax
import jax.numpy as jnp
from jax import lax
from jax.experimental import pallas as pl
from jax.experimental.pallas import tpu as pltpu
from jax.sharding import Mesh, PartitionSpec as P


def with_halo(block, sides, width):
    for axis, dim in sides:
        count = lax.axis_size(axis)
        forward = [(i, i + 1) for i in range(count - 1)]
        backward = [(target, source) for source, target in forward]
        low = lax.ppermute(
            lax.slice_in_dim(block, block.shape[dim] - width, None, axis=dim), axis, forward
        )
        high = lax.ppermute(lax.slice_in_dim(block, 0, width, axis=dim), axis, backward)
        block = jnp.concatenate([low, block, high], axis=dim)
    return block


ROW = ("rzy", "core")


def per_device(b_tiles, occ_coeff, tile_blocks, screen_mask):
    p_local, rows_local, stored = b_tiles.shape
    blocks_local, slot_count = tile_blocks.shape
    block_size = rows_local // blocks_local
    orbitals = occ_coeff.shape[1]
    aux_count = lax.axis_size("aux")
    row_index = lax.axis_index(ROW)
    extended = with_halo(occ_coeff, ((ROW, 0),), rows_local)
    coeff_blocks = extended.reshape(3 * blocks_local, block_size, orbitals)
    local_index = tile_blocks - (row_index - 1) * blocks_local
    window = coeff_blocks.shape[0]
    local_index = jnp.clip(local_index, 0, window - 1).astype(jnp.int32)
    tiles = b_tiles.reshape(rows_local, stored)
    extended = extended.reshape(window * block_size, orbitals)

    def kernel(index_ref, mask_ref, tile_ref, coeff_ref, out_ref):
        b = pl.program_id(0)
        acc = jnp.zeros(out_ref.shape, jnp.float32)
        for s in range(slot_count):
            start = pl.multiple_of(index_ref[b, s] * block_size, block_size)
            coeff = coeff_ref[pl.ds(start, block_size), :]
            coeff = jnp.where(mask_ref[b, s] != 0, coeff, jnp.zeros_like(coeff))
            tile = tile_ref[:, s * block_size:(s + 1) * block_size]
            acc = acc + jnp.dot(tile, coeff, preferred_element_type=jnp.float32)
        out_ref[...] = acc.astype(out_ref.dtype)

    half_local = pl.pallas_call(
        kernel,
        grid_spec=pltpu.PrefetchScalarGridSpec(
            num_scalar_prefetch=2,
            grid=(blocks_local,),
            in_specs=[
                pl.BlockSpec((block_size, stored), lambda b, li, mk: (b, 0)),
                pl.BlockSpec((window * block_size, orbitals), lambda b, li, mk: (0, 0)),
            ],
            out_specs=pl.BlockSpec((block_size, orbitals), lambda b, li, mk: (b, 0)),
        ),
        out_shape=jax.ShapeDtypeStruct((rows_local, orbitals), jnp.bfloat16),
    )(local_index, screen_mask, tiles, extended)
    half_local = half_local.reshape(p_local, rows_local, orbitals)
    aux_index = lax.axis_index("aux")
    share = rows_local // aux_count
    own = half_local[0]
    pieces = [lax.dynamic_slice_in_dim(own, aux_index * share, share, axis=0)]
    shifted = [own]
    for shift in range(1, aux_count):
        pairs = [(i, (i + shift) % aux_count) for i in range(aux_count)]
        target = (aux_index + shift) % aux_count
        outgoing = lax.dynamic_slice_in_dim(own, target * share, share, axis=0)
        pieces.append(lax.ppermute(outgoing, "aux", pairs))
        shifted.append(lax.ppermute(own, "aux", pairs))
    piece = jnp.stack(pieces)
    slab_rows = jnp.stack(shifted)
    partner = lax.all_gather(piece, ROW, axis=0)
    result = jnp.einsum("pmi,rpki->mrk", slab_rows, partner, preferred_element_type=jnp.float32)
    return result.astype(jnp.bfloat16).reshape(rows_local, partner.shape[0], 1, share)


def solution(mesh):
    aux_count, row_count = mesh.devices.shape
    devices = mesh.devices.reshape(aux_count, row_count // 2, 2)
    split_mesh = Mesh(devices, ("aux",) + ROW)
    in_specs = (P("aux", ROW, None), P(ROW, None), P(ROW, None), P(ROW, None))
    out_specs = P(ROW, None, "aux", None)
    return jax.shard_map(
        per_device, mesh=split_mesh, in_specs=in_specs, out_specs=out_specs, check_vma=False
    )
```

```python
import jax
import jax.numpy as jnp
from jax import lax
from jax.experimental import pallas as pl
from jax.experimental.pallas import tpu as pltpu
from jax.sharding import Mesh, PartitionSpec as P


def halo_pieces(block, axis, width):
    count = lax.axis_size(axis)
    forward = [(i, i + 1) for i in range(count - 1)]
    backward = [(target, source) for source, target in forward]
    low = lax.ppermute(lax.slice_in_dim(block, block.shape[0] - width, None, axis=0), axis, forward)
    high = lax.ppermute(lax.slice_in_dim(block, 0, width, axis=0), axis, backward)
    return low, high


ROW = ("rzy", "core")


def per_device(b_tiles, occ_coeff, tile_blocks, screen_mask):
    p_local, rows_local, stored = b_tiles.shape
    blocks_local, slot_count = tile_blocks.shape
    block_size = rows_local // blocks_local
    orbitals = occ_coeff.shape[1]
    aux_count = lax.axis_size("aux")
    row_index = lax.axis_index(ROW)
    low, high = halo_pieces(occ_coeff, ROW, rows_local)
    window = 3 * blocks_local
    local_index = tile_blocks - (row_index - 1) * blocks_local
    local_index = jnp.clip(local_index, 0, window - 1).astype(jnp.int32)
    tiles = b_tiles.reshape(rows_local, stored)

    def kernel(index_ref, mask_ref, tile_ref, low_ref, own_ref, high_ref, out_ref, coeff_ref, rhs_ref):
        b = pl.program_id(0)

        @pl.when(b == 0)
        def _():
            coeff_ref[0:rows_local, :] = low_ref[...]
            coeff_ref[rows_local:2 * rows_local, :] = own_ref[...]
            coeff_ref[2 * rows_local:3 * rows_local, :] = high_ref[...]

        for s in range(slot_count):
            start = pl.multiple_of(index_ref[b, s] * block_size, block_size)
            coeff = coeff_ref[pl.ds(start, block_size), :]
            coeff = jnp.where(mask_ref[b, s] != 0, coeff, jnp.zeros_like(coeff))
            rhs_ref[s * block_size:(s + 1) * block_size, :] = coeff
        acc = jnp.dot(tile_ref[...], rhs_ref[...], preferred_element_type=jnp.float32)
        out_ref[...] = acc.astype(out_ref.dtype)

    whole = pl.BlockSpec((rows_local, orbitals), lambda b, li, mk: (0, 0))
    half_local = pl.pallas_call(
        kernel,
        grid_spec=pltpu.PrefetchScalarGridSpec(
            num_scalar_prefetch=2,
            grid=(blocks_local,),
            in_specs=[
                pl.BlockSpec((block_size, stored), lambda b, li, mk: (b, 0)),
                whole,
                whole,
                whole,
            ],
            out_specs=pl.BlockSpec((block_size, orbitals), lambda b, li, mk: (b, 0)),
            scratch_shapes=[
                pltpu.VMEM((window * block_size, orbitals), occ_coeff.dtype),
                pltpu.VMEM((stored, orbitals), occ_coeff.dtype),
            ],
        ),
        out_shape=jax.ShapeDtypeStruct((rows_local, orbitals), jnp.bfloat16),
        compiler_params=pltpu.CompilerParams(dimension_semantics=("arbitrary",)),
    )(local_index, screen_mask, tiles, low, occ_coeff, high)
    half_local = half_local.reshape(p_local, rows_local, orbitals)
    aux_index = lax.axis_index("aux")
    share = rows_local // aux_count
    own = half_local[0]
    pieces = [lax.dynamic_slice_in_dim(own, aux_index * share, share, axis=0)]
    shifted = [own]
    for shift in range(1, aux_count):
        pairs = [(i, (i + shift) % aux_count) for i in range(aux_count)]
        target = (aux_index + shift) % aux_count
        outgoing = lax.dynamic_slice_in_dim(own, target * share, share, axis=0)
        pieces.append(lax.ppermute(outgoing, "aux", pairs))
        shifted.append(lax.ppermute(own, "aux", pairs))
    piece = jnp.stack(pieces)
    slab_rows = jnp.stack(shifted)
    partner = lax.all_gather(piece, ROW, axis=0)
    result = jnp.einsum("pmi,rpki->mrk", slab_rows, partner, preferred_element_type=jnp.float32)
    return result.astype(jnp.bfloat16).reshape(rows_local, partner.shape[0], 1, share)


def solution(mesh):
    aux_count, row_count = mesh.devices.shape
    devices = mesh.devices.reshape(aux_count, row_count // 2, 2)
    split_mesh = Mesh(devices, ("aux",) + ROW)
    in_specs = (P("aux", ROW, None), P(ROW, None), P(ROW, None), P(ROW, None))
    out_specs = P(ROW, None, "aux", None)
    return jax.shard_map(
        per_device, mesh=split_mesh, in_specs=in_specs, out_specs=out_specs, check_vma=False
    )
```

```python
import jax
import jax.numpy as jnp
from jax import lax
from jax.experimental import pallas as pl
from jax.experimental.pallas import tpu as pltpu
from jax.sharding import Mesh, PartitionSpec as P


def halo_pieces(block, axis, width):
    count = lax.axis_size(axis)
    forward = [(i, i + 1) for i in range(count - 1)]
    backward = [(target, source) for source, target in forward]
    low = lax.ppermute(lax.slice_in_dim(block, block.shape[0] - width, None, axis=0), axis, forward)
    high = lax.ppermute(lax.slice_in_dim(block, 0, width, axis=0), axis, backward)
    return low, high


ROW = ("rzy", "core")


def per_device(b_tiles, occ_coeff, tile_blocks, screen_mask):
    p_local, rows_local, stored = b_tiles.shape
    blocks_local, slot_count = tile_blocks.shape
    block_size = rows_local // blocks_local
    orbitals = occ_coeff.shape[1]
    aux_count = lax.axis_size("aux")
    row_index = lax.axis_index(ROW)
    low, high = halo_pieces(occ_coeff, ROW, rows_local)
    window = 3 * blocks_local
    local_index = tile_blocks - (row_index - 1) * blocks_local
    local_index = jnp.clip(local_index, 0, window - 1).astype(jnp.int32)
    tiles = b_tiles.reshape(rows_local, stored)

    def kernel(index_ref, mask_ref, tile_ref, low_ref, own_ref, high_ref, out_ref, coeff_ref, rhs_ref):
        b = pl.program_id(0)

        @pl.when(b == 0)
        def _():
            coeff_ref[0:rows_local, :] = low_ref[...]
            coeff_ref[rows_local:2 * rows_local, :] = own_ref[...]
            coeff_ref[2 * rows_local:3 * rows_local, :] = high_ref[...]

        for s in range(slot_count):
            start = pl.multiple_of(index_ref[b, s] * block_size, block_size)
            coeff = coeff_ref[pl.ds(start, block_size), :]
            coeff = jnp.where(mask_ref[b, s] != 0, coeff, jnp.zeros_like(coeff))
            rhs_ref[s * block_size:(s + 1) * block_size, :] = coeff
        acc = jnp.dot(tile_ref[...], rhs_ref[...], preferred_element_type=jnp.float32)
        out_ref[...] = acc.astype(out_ref.dtype)

    whole = pl.BlockSpec((rows_local, orbitals), lambda b, li, mk: (0, 0))
    half_local = pl.pallas_call(
        kernel,
        grid_spec=pltpu.PrefetchScalarGridSpec(
            num_scalar_prefetch=2,
            grid=(blocks_local,),
            in_specs=[
                pl.BlockSpec((block_size, stored), lambda b, li, mk: (b, 0)),
                whole,
                whole,
                whole,
            ],
            out_specs=pl.BlockSpec((block_size, orbitals), lambda b, li, mk: (b, 0)),
            scratch_shapes=[
                pltpu.VMEM((window * block_size, orbitals), occ_coeff.dtype),
                pltpu.VMEM((stored, orbitals), occ_coeff.dtype),
            ],
        ),
        out_shape=jax.ShapeDtypeStruct((rows_local, orbitals), jnp.bfloat16),
        compiler_params=pltpu.CompilerParams(dimension_semantics=("arbitrary",)),
    )(local_index, screen_mask, tiles, low, occ_coeff, high)
    half_local = half_local.reshape(p_local, rows_local, orbitals)
    aux_index = lax.axis_index("aux")
    share = rows_local // aux_count
    own = half_local[0]
    pieces = [lax.dynamic_slice_in_dim(own, aux_index * share, share, axis=0)]
    shifted = [own]
    for shift in range(1, aux_count):
        pairs = [(i, (i + shift) % aux_count) for i in range(aux_count)]
        target = (aux_index + shift) % aux_count
        outgoing = lax.dynamic_slice_in_dim(own, target * share, share, axis=0)
        pieces.append(lax.ppermute(outgoing, "aux", pairs))
        shifted.append(lax.ppermute(own, "aux", pairs))
    piece = jnp.stack(pieces)
    slab_rows = jnp.stack(shifted)
    partner = lax.all_gather(piece, ROW, axis=0)
    result = jnp.einsum("pmi,rpki->rmk", slab_rows, partner, preferred_element_type=jnp.float32)
    result = result.astype(jnp.bfloat16)
    row_count = partner.shape[0]
    rows_tile = 64

    def relayout(in_ref, out_ref):
        x = in_ref[...].astype(jnp.float32)
        out_ref[...] = pltpu.einshape("rmk->mrk", x).astype(out_ref.dtype)

    result = pl.pallas_call(
        relayout,
        grid=(rows_local // rows_tile,),
        in_specs=[pl.BlockSpec((row_count, rows_tile, share), lambda i: (0, i, 0))],
        out_specs=pl.BlockSpec((rows_tile, row_count, share), lambda i: (i, 0, 0)),
        out_shape=jax.ShapeDtypeStruct((rows_local, row_count, share), jnp.bfloat16),
    )(result)
    return result.reshape(rows_local, row_count, 1, share)


def solution(mesh):
    aux_count, row_count = mesh.devices.shape
    devices = mesh.devices.reshape(aux_count, row_count // 2, 2)
    split_mesh = Mesh(devices, ("aux",) + ROW)
    in_specs = (P("aux", ROW, None), P(ROW, None), P(ROW, None), P(ROW, None))
    out_specs = P(ROW, None, "aux", None)
    return jax.shard_map(
        per_device, mesh=split_mesh, in_specs=in_specs, out_specs=out_specs, check_vma=False
    )
```

```python
import jax
import jax.numpy as jnp
from jax import lax
from jax.experimental import pallas as pl
from jax.experimental.pallas import tpu as pltpu
from jax.sharding import Mesh, PartitionSpec as P


def halo_pieces(block, axis, width):
    count = lax.axis_size(axis)
    forward = [(i, i + 1) for i in range(count - 1)]
    backward = [(target, source) for source, target in forward]
    low = lax.ppermute(lax.slice_in_dim(block, block.shape[0] - width, None, axis=0), axis, forward)
    high = lax.ppermute(lax.slice_in_dim(block, 0, width, axis=0), axis, backward)
    return low, high


ROW = ("rzy", "core")


def per_device(b_tiles, occ_coeff, tile_blocks, screen_mask):
    p_local, rows_local, stored = b_tiles.shape
    blocks_local, slot_count = tile_blocks.shape
    block_size = rows_local // blocks_local
    orbitals = occ_coeff.shape[1]
    aux_count = lax.axis_size("aux")
    row_index = lax.axis_index(ROW)
    low, high = halo_pieces(occ_coeff, ROW, rows_local)
    window = 3 * blocks_local
    local_index = tile_blocks - (row_index - 1) * blocks_local
    local_index = jnp.clip(local_index, 0, window - 1).astype(jnp.int32)
    tiles = b_tiles.reshape(rows_local, stored)

    def kernel(index_ref, mask_ref, tile_ref, low_ref, own_ref, high_ref, out_ref, coeff_ref, rhs_ref):
        b = pl.program_id(0)

        @pl.when(b == 0)
        def _():
            coeff_ref[0:rows_local, :] = low_ref[...]
            coeff_ref[rows_local:2 * rows_local, :] = own_ref[...]
            coeff_ref[2 * rows_local:3 * rows_local, :] = high_ref[...]

        for s in range(slot_count):
            start = pl.multiple_of(index_ref[b, s] * block_size, block_size)
            coeff = coeff_ref[pl.ds(start, block_size), :]
            coeff = jnp.where(mask_ref[b, s] != 0, coeff, jnp.zeros_like(coeff))
            rhs_ref[s * block_size:(s + 1) * block_size, :] = coeff
        acc = jnp.dot(tile_ref[...], rhs_ref[...], preferred_element_type=jnp.float32)
        out_ref[...] = acc.astype(out_ref.dtype)

    whole = pl.BlockSpec((rows_local, orbitals), lambda b, li, mk: (0, 0))
    half_local = pl.pallas_call(
        kernel,
        grid_spec=pltpu.PrefetchScalarGridSpec(
            num_scalar_prefetch=2,
            grid=(blocks_local,),
            in_specs=[
                pl.BlockSpec((block_size, stored), lambda b, li, mk: (b, 0)),
                whole,
                whole,
                whole,
            ],
            out_specs=pl.BlockSpec((block_size, orbitals), lambda b, li, mk: (b, 0)),
            scratch_shapes=[
                pltpu.VMEM((window * block_size, orbitals), occ_coeff.dtype),
                pltpu.VMEM((stored, orbitals), occ_coeff.dtype),
            ],
        ),
        out_shape=jax.ShapeDtypeStruct((rows_local, orbitals), jnp.bfloat16),
        compiler_params=pltpu.CompilerParams(dimension_semantics=("arbitrary",)),
    )(local_index, screen_mask, tiles, low, occ_coeff, high)
    half_local = half_local.reshape(p_local, rows_local, orbitals)
    aux_index = lax.axis_index("aux")
    share = rows_local // aux_count
    own = half_local[0]
    shifted = [own]
    for shift in range(1, aux_count):
        pairs = [(i, (i + shift) % aux_count) for i in range(aux_count)]
        shifted.append(lax.ppermute(own, "aux", pairs))
    piece = lax.all_to_all(
        own.reshape(aux_count, share, orbitals), "aux", 0, 0, tiled=True
    )
    order = (aux_index - jnp.arange(aux_count)) % aux_count
    slab_rows = jnp.take(jnp.stack(shifted), order, axis=0)
    partner = lax.all_gather(piece, ROW, axis=0)
    result = jnp.einsum("pmi,rpki->mrk", slab_rows, partner, preferred_element_type=jnp.float32)
    return result.astype(jnp.bfloat16).reshape(rows_local, partner.shape[0], 1, share)


def solution(mesh):
    aux_count, row_count = mesh.devices.shape
    devices = mesh.devices.reshape(aux_count, row_count // 2, 2)
    split_mesh = Mesh(devices, ("aux",) + ROW)
    in_specs = (P("aux", ROW, None), P(ROW, None), P(ROW, None), P(ROW, None))
    out_specs = P(ROW, None, "aux", None)
    return jax.shard_map(
        per_device, mesh=split_mesh, in_specs=in_specs, out_specs=out_specs, check_vma=False
    )
```

```python
import jax
import jax.numpy as jnp
from jax import lax
from jax.experimental import pallas as pl
from jax.experimental.pallas import tpu as pltpu
from jax.sharding import Mesh, PartitionSpec as P


def halo_pieces(block, axis, width):
    count = lax.axis_size(axis)
    forward = [(i, i + 1) for i in range(count - 1)]
    backward = [(target, source) for source, target in forward]
    low = lax.ppermute(lax.slice_in_dim(block, block.shape[0] - width, None, axis=0), axis, forward)
    high = lax.ppermute(lax.slice_in_dim(block, 0, width, axis=0), axis, backward)
    return low, high


ROW = ("rzy", "core")


def per_device(b_tiles, occ_coeff, tile_blocks, screen_mask):
    p_local, rows_local, stored = b_tiles.shape
    blocks_local, slot_count = tile_blocks.shape
    block_size = rows_local // blocks_local
    orbitals = occ_coeff.shape[1]
    aux_count = lax.axis_size("aux")
    row_index = lax.axis_index(ROW)
    low, high = halo_pieces(occ_coeff, ROW, rows_local)
    window = 3 * blocks_local
    local_index = tile_blocks - (row_index - 1) * blocks_local
    local_index = jnp.clip(local_index, 0, window - 1).astype(jnp.int32)
    tiles = b_tiles.reshape(rows_local, stored)

    quarters = 4
    quarter = stored // quarters

    def kernel(index_ref, mask_ref, *refs):
        tile_refs = refs[:quarters]
        low_ref, own_ref, high_ref, out_ref, coeff_ref, rhs_ref = refs[quarters:]
        b = pl.program_id(0)

        @pl.when(b == 0)
        def _():
            coeff_ref[0:rows_local, :] = low_ref[...]
            coeff_ref[rows_local:2 * rows_local, :] = own_ref[...]
            coeff_ref[2 * rows_local:3 * rows_local, :] = high_ref[...]

        for s in range(slot_count):
            start = pl.multiple_of(index_ref[b, s] * block_size, block_size)
            coeff = coeff_ref[pl.ds(start, block_size), :]
            coeff = jnp.where(mask_ref[b, s] != 0, coeff, jnp.zeros_like(coeff))
            rhs_ref[s * block_size:(s + 1) * block_size, :] = coeff
        acc = jnp.zeros(out_ref.shape, jnp.float32)
        for q in range(quarters):
            rhs = rhs_ref[q * quarter:(q + 1) * quarter, :]
            acc = acc + jnp.dot(tile_refs[q][...], rhs, preferred_element_type=jnp.float32)
        out_ref[...] = acc.astype(out_ref.dtype)

    whole = pl.BlockSpec((rows_local, orbitals), lambda b, li, mk: (0, 0))
    half_local = pl.pallas_call(
        kernel,
        grid_spec=pltpu.PrefetchScalarGridSpec(
            num_scalar_prefetch=2,
            grid=(blocks_local,),
            in_specs=[
                pl.BlockSpec((block_size, quarter), lambda b, li, mk, q=q: (b, q))
                for q in range(quarters)
            ]
            + [
                whole,
                whole,
                whole,
            ],
            out_specs=pl.BlockSpec((block_size, orbitals), lambda b, li, mk: (b, 0)),
            scratch_shapes=[
                pltpu.VMEM((window * block_size, orbitals), occ_coeff.dtype),
                pltpu.VMEM((stored, orbitals), occ_coeff.dtype),
            ],
        ),
        out_shape=jax.ShapeDtypeStruct((rows_local, orbitals), jnp.bfloat16),
        compiler_params=pltpu.CompilerParams(dimension_semantics=("arbitrary",)),
    )(local_index, screen_mask, *([tiles] * quarters), low, occ_coeff, high)
    half_local = half_local.reshape(p_local, rows_local, orbitals)
    aux_index = lax.axis_index("aux")
    share = rows_local // aux_count
    own = half_local[0]
    shifted = [own]
    for shift in range(1, aux_count):
        pairs = [(i, (i + shift) % aux_count) for i in range(aux_count)]
        shifted.append(lax.ppermute(own, "aux", pairs))
    piece = lax.all_to_all(
        own.reshape(aux_count, share, orbitals), "aux", 0, 0, tiled=True
    )
    order = (aux_index - jnp.arange(aux_count)) % aux_count
    slab_rows = jnp.take(jnp.stack(shifted), order, axis=0)
    partner = lax.all_gather(piece, ROW, axis=0)
    result = jnp.einsum("pmi,rpki->mrk", slab_rows, partner, preferred_element_type=jnp.float32)
    return result.astype(jnp.bfloat16).reshape(rows_local, partner.shape[0], 1, share)


def solution(mesh):
    aux_count, row_count = mesh.devices.shape
    devices = mesh.devices.reshape(aux_count, row_count // 2, 2)
    split_mesh = Mesh(devices, ("aux",) + ROW)
    in_specs = (P("aux", ROW, None), P(ROW, None), P(ROW, None), P(ROW, None))
    out_specs = P(ROW, None, "aux", None)
    return jax.shard_map(
        per_device, mesh=split_mesh, in_specs=in_specs, out_specs=out_specs, check_vma=False
    )
```

```python
import jax
import jax.numpy as jnp
from jax import lax
from jax.experimental import pallas as pl
from jax.experimental.pallas import tpu as pltpu
from jax.sharding import Mesh, PartitionSpec as P


def halo_pieces(block, axis, width):
    count = lax.axis_size(axis)
    forward = [(i, i + 1) for i in range(count - 1)]
    backward = [(target, source) for source, target in forward]
    low = lax.ppermute(lax.slice_in_dim(block, block.shape[0] - width, None, axis=0), axis, forward)
    high = lax.ppermute(lax.slice_in_dim(block, 0, width, axis=0), axis, backward)
    return low, high


ROW = ("rzy", "core")


def per_device(b_tiles, occ_coeff, tile_blocks, screen_mask):
    p_local, rows_local, stored = b_tiles.shape
    blocks_local, slot_count = tile_blocks.shape
    block_size = rows_local // blocks_local
    orbitals = occ_coeff.shape[1]
    aux_count = lax.axis_size("aux")
    row_index = lax.axis_index(ROW)
    low, high = halo_pieces(occ_coeff, ROW, rows_local)
    window = 3 * blocks_local
    local_index = tile_blocks - (row_index - 1) * blocks_local
    local_index = jnp.clip(local_index, 0, window - 1).astype(jnp.int32)
    tiles = b_tiles.reshape(rows_local, stored)

    quarters = 4
    quarter = stored // quarters

    def kernel(index_ref, mask_ref, *refs):
        tile_refs = refs[:quarters]
        low_ref, own_ref, high_ref, out_ref, coeff_ref, rhs_ref = refs[quarters:]
        b = pl.program_id(0)

        @pl.when(b == 0)
        def _():
            coeff_ref[0:rows_local, :] = low_ref[...]
            coeff_ref[rows_local:2 * rows_local, :] = own_ref[...]
            coeff_ref[2 * rows_local:3 * rows_local, :] = high_ref[...]

        for s in range(slot_count):
            start = pl.multiple_of(index_ref[b, s] * block_size, block_size)
            coeff = coeff_ref[pl.ds(start, block_size), :]
            coeff = jnp.where(mask_ref[b, s] != 0, coeff, jnp.zeros_like(coeff))
            rhs_ref[s * block_size:(s + 1) * block_size, :] = coeff
        acc = jnp.zeros(out_ref.shape, jnp.float32)
        for q in range(quarters):
            rhs = rhs_ref[q * quarter:(q + 1) * quarter, :]
            acc = acc + jnp.dot(tile_refs[q][...], rhs, preferred_element_type=jnp.float32)
        out_ref[...] = acc.astype(out_ref.dtype)

    whole = pl.BlockSpec((rows_local, orbitals), lambda b, li, mk: (0, 0))
    half_local = pl.pallas_call(
        kernel,
        grid_spec=pltpu.PrefetchScalarGridSpec(
            num_scalar_prefetch=2,
            grid=(blocks_local,),
            in_specs=[
                pl.BlockSpec((block_size, quarter), lambda b, li, mk, q=q: (b, q))
                for q in range(quarters)
            ]
            + [
                whole,
                whole,
                whole,
            ],
            out_specs=pl.BlockSpec((block_size, orbitals), lambda b, li, mk: (b, 0)),
            scratch_shapes=[
                pltpu.VMEM((window * block_size, orbitals), occ_coeff.dtype),
                pltpu.VMEM((stored, orbitals), occ_coeff.dtype),
            ],
        ),
        out_shape=jax.ShapeDtypeStruct((rows_local, orbitals), jnp.bfloat16),
        compiler_params=pltpu.CompilerParams(dimension_semantics=("arbitrary",)),
    )(local_index, screen_mask, *([tiles] * quarters), low, occ_coeff, high)
    half_local = half_local.reshape(p_local, rows_local, orbitals)
    aux_index = lax.axis_index("aux")
    share = rows_local // aux_count
    own = half_local[0]
    shifted = [own]
    for shift in range(1, aux_count):
        pairs = [(i, (i + shift) % aux_count) for i in range(aux_count)]
        shifted.append(lax.ppermute(own, "aux", pairs))
    piece = lax.all_to_all(
        own.reshape(aux_count, share, orbitals), "aux", 0, 0, tiled=True
    )
    order = (aux_index - jnp.arange(aux_count)) % aux_count
    slab_rows = jnp.take(jnp.stack(shifted), order, axis=0)
    piece = jnp.transpose(piece, (1, 0, 2))
    partner = lax.all_gather(piece, ROW, axis=0)
    row_count = partner.shape[0]
    partner = partner.reshape(row_count * share, aux_count * orbitals)
    slab_rows = jnp.transpose(slab_rows, (1, 0, 2)).reshape(rows_local, aux_count * orbitals)
    result = jnp.einsum("mq,lq->ml", slab_rows, partner, preferred_element_type=jnp.float32)
    return result.astype(jnp.bfloat16).reshape(rows_local, row_count, 1, share)


def solution(mesh):
    aux_count, row_count = mesh.devices.shape
    devices = mesh.devices.reshape(aux_count, row_count // 2, 2)
    split_mesh = Mesh(devices, ("aux",) + ROW)
    in_specs = (P("aux", ROW, None), P(ROW, None), P(ROW, None), P(ROW, None))
    out_specs = P(ROW, None, "aux", None)
    return jax.shard_map(
        per_device, mesh=split_mesh, in_specs=in_specs, out_specs=out_specs, check_vma=False
    )
```

```python
import jax
import jax.numpy as jnp
from jax import lax
from jax.experimental import pallas as pl
from jax.experimental.pallas import tpu as pltpu
from jax.sharding import Mesh, PartitionSpec as P


def halo_pieces(block, axis, width):
    count = lax.axis_size(axis)
    forward = [(i, i + 1) for i in range(count - 1)]
    backward = [(target, source) for source, target in forward]
    low = lax.ppermute(lax.slice_in_dim(block, block.shape[0] - width, None, axis=0), axis, forward)
    high = lax.ppermute(lax.slice_in_dim(block, 0, width, axis=0), axis, backward)
    return low, high


ROW = ("rzy", "core")


def per_device(b_tiles, occ_coeff, tile_blocks, screen_mask):
    p_local, rows_local, stored = b_tiles.shape
    blocks_local, slot_count = tile_blocks.shape
    block_size = rows_local // blocks_local
    orbitals = occ_coeff.shape[1]
    aux_count = lax.axis_size("aux")
    row_index = lax.axis_index(ROW)
    low, high = halo_pieces(occ_coeff, ROW, rows_local)
    window = 3 * blocks_local
    local_index = tile_blocks - (row_index - 1) * blocks_local
    local_index = jnp.clip(local_index, 0, window - 1).astype(jnp.int32)
    tiles = b_tiles.reshape(rows_local, stored)

    quarters = 4
    quarter = stored // quarters

    def kernel(index_ref, mask_ref, *refs):
        tile_refs = refs[:quarters]
        low_ref, own_ref, high_ref, out_ref, coeff_ref, rhs_ref = refs[quarters:]
        b = pl.program_id(0)

        @pl.when(b == 0)
        def _():
            coeff_ref[0:rows_local, :] = low_ref[...]
            coeff_ref[rows_local:2 * rows_local, :] = own_ref[...]
            coeff_ref[2 * rows_local:3 * rows_local, :] = high_ref[...]

        for s in range(slot_count):
            start = pl.multiple_of(index_ref[b, s] * block_size, block_size)
            coeff = coeff_ref[pl.ds(start, block_size), :]
            coeff = jnp.where(mask_ref[b, s] != 0, coeff, jnp.zeros_like(coeff))
            rhs_ref[s * block_size:(s + 1) * block_size, :] = coeff
        acc = jnp.zeros(out_ref.shape, jnp.float32)
        for q in range(quarters):
            rhs = rhs_ref[q * quarter:(q + 1) * quarter, :]
            acc = acc + jnp.dot(tile_refs[q][...], rhs, preferred_element_type=jnp.float32)
        out_ref[...] = acc.astype(out_ref.dtype)

    whole = pl.BlockSpec((rows_local, orbitals), lambda b, li, mk: (0, 0))
    half_local = pl.pallas_call(
        kernel,
        grid_spec=pltpu.PrefetchScalarGridSpec(
            num_scalar_prefetch=2,
            grid=(blocks_local,),
            in_specs=[
                pl.BlockSpec((block_size, quarter), lambda b, li, mk, q=q: (b, q))
                for q in range(quarters)
            ]
            + [
                whole,
                whole,
                whole,
            ],
            out_specs=pl.BlockSpec((block_size, orbitals), lambda b, li, mk: (b, 0)),
            scratch_shapes=[
                pltpu.VMEM((window * block_size, orbitals), occ_coeff.dtype),
                pltpu.VMEM((stored, orbitals), occ_coeff.dtype),
            ],
        ),
        out_shape=jax.ShapeDtypeStruct((rows_local, orbitals), jnp.bfloat16),
        compiler_params=pltpu.CompilerParams(dimension_semantics=("arbitrary",)),
    )(local_index, screen_mask, *([tiles] * quarters), low, occ_coeff, high)
    half_local = half_local.reshape(p_local, rows_local, orbitals)
    aux_index = lax.axis_index("aux")
    share = rows_local // aux_count
    own = half_local[0]
    shifted = [own]
    for shift in range(1, aux_count):
        pairs = [(i, (i + shift) % aux_count) for i in range(aux_count)]
        shifted.append(lax.ppermute(own, "aux", pairs))
    piece = lax.all_to_all(
        own.reshape(aux_count, share, orbitals), "aux", 0, 0, tiled=True
    )
    order = (aux_index - jnp.arange(aux_count)) % aux_count
    slab_rows = jnp.take(jnp.stack(shifted), order, axis=0)
    partner = lax.all_gather(piece, ROW, axis=0)
    result = jnp.einsum("pmi,rpki->rmk", slab_rows, partner, preferred_element_type=jnp.float32)
    result = result.astype(jnp.bfloat16)
    row_count = partner.shape[0]
    rows_tile = 64

    def relayout(in_ref, out_ref):
        out_ref[...] = pltpu.einshape("rmk->mrk", in_ref[...])

    result = pl.pallas_call(
        relayout,
        grid=(rows_local // rows_tile,),
        in_specs=[pl.BlockSpec((row_count, rows_tile, share), lambda i: (0, i, 0))],
        out_specs=pl.BlockSpec((rows_tile, row_count, share), lambda i: (i, 0, 0)),
        out_shape=jax.ShapeDtypeStruct((rows_local, row_count, share), jnp.bfloat16),
    )(result)
    return result.reshape(rows_local, row_count, 1, share)


def solution(mesh):
    aux_count, row_count = mesh.devices.shape
    devices = mesh.devices.reshape(aux_count, row_count // 2, 2)
    split_mesh = Mesh(devices, ("aux",) + ROW)
    in_specs = (P("aux", ROW, None), P(ROW, None), P(ROW, None), P(ROW, None))
    out_specs = P(ROW, None, "aux", None)
    return jax.shard_map(
        per_device, mesh=split_mesh, in_specs=in_specs, out_specs=out_specs, check_vma=False
    )
```

```python
import jax
import jax.numpy as jnp
from jax import lax
from jax.experimental import pallas as pl
from jax.experimental.pallas import tpu as pltpu
from jax.sharding import Mesh, PartitionSpec as P


def halo_pieces(block, axis, width):
    count = lax.axis_size(axis)
    forward = [(i, i + 1) for i in range(count - 1)]
    backward = [(target, source) for source, target in forward]
    low = lax.ppermute(lax.slice_in_dim(block, block.shape[0] - width, None, axis=0), axis, forward)
    high = lax.ppermute(lax.slice_in_dim(block, 0, width, axis=0), axis, backward)
    return low, high


ROW = ("rzy", "core")


def per_device(b_tiles, occ_coeff, tile_blocks, screen_mask):
    p_local, rows_local, stored = b_tiles.shape
    blocks_local, slot_count = tile_blocks.shape
    block_size = rows_local // blocks_local
    orbitals = occ_coeff.shape[1]
    aux_count = lax.axis_size("aux")
    row_index = lax.axis_index(ROW)
    low, high = halo_pieces(occ_coeff, ROW, rows_local)
    window = 3 * blocks_local
    local_index = tile_blocks - (row_index - 1) * blocks_local
    local_index = jnp.clip(local_index, 0, window - 1).astype(jnp.int32)
    tiles = b_tiles.reshape(rows_local, stored)

    quarters = 4
    quarter = stored // quarters

    def kernel(index_ref, mask_ref, *refs):
        tile_refs = refs[:quarters]
        low_ref, own_ref, high_ref, out_ref, coeff_ref, rhs_ref = refs[quarters:]
        b = pl.program_id(0)

        @pl.when(b == 0)
        def _():
            coeff_ref[0:rows_local, :] = low_ref[...]
            coeff_ref[rows_local:2 * rows_local, :] = own_ref[...]
            coeff_ref[2 * rows_local:3 * rows_local, :] = high_ref[...]

        for s in range(slot_count):
            start = pl.multiple_of(index_ref[b, s] * block_size, block_size)
            coeff = coeff_ref[pl.ds(start, block_size), :]
            coeff = jnp.where(mask_ref[b, s] != 0, coeff, jnp.zeros_like(coeff))
            rhs_ref[s * block_size:(s + 1) * block_size, :] = coeff
        acc = jnp.zeros(out_ref.shape, jnp.float32)
        for q in range(quarters):
            rhs = rhs_ref[q * quarter:(q + 1) * quarter, :]
            acc = acc + jnp.dot(tile_refs[q][...], rhs, preferred_element_type=jnp.float32)
        out_ref[...] = acc.astype(out_ref.dtype)

    whole = pl.BlockSpec((rows_local, orbitals), lambda b, li, mk: (0, 0))
    half_local = pl.pallas_call(
        kernel,
        grid_spec=pltpu.PrefetchScalarGridSpec(
            num_scalar_prefetch=2,
            grid=(blocks_local,),
            in_specs=[
                pl.BlockSpec((block_size, quarter), lambda b, li, mk, q=q: (b, q))
                for q in range(quarters)
            ]
            + [
                whole,
                whole,
                whole,
            ],
            out_specs=pl.BlockSpec((block_size, orbitals), lambda b, li, mk: (b, 0)),
            scratch_shapes=[
                pltpu.VMEM((window * block_size, orbitals), occ_coeff.dtype),
                pltpu.VMEM((stored, orbitals), occ_coeff.dtype),
            ],
        ),
        out_shape=jax.ShapeDtypeStruct((rows_local, orbitals), jnp.bfloat16),
        compiler_params=pltpu.CompilerParams(dimension_semantics=("arbitrary",)),
    )(local_index, screen_mask, *([tiles] * quarters), low, occ_coeff, high)
    half_local = half_local.reshape(p_local, rows_local, orbitals)
    aux_index = lax.axis_index("aux")
    share = rows_local // aux_count
    own = half_local[0]
    shifted = [own]
    for shift in range(1, aux_count):
        pairs = [(i, (i + shift) % aux_count) for i in range(aux_count)]
        shifted.append(lax.ppermute(own, "aux", pairs))
    piece = lax.all_to_all(
        own.reshape(aux_count, share, orbitals), "aux", 0, 0, tiled=True
    )
    order = (aux_index - jnp.arange(aux_count)) % aux_count
    slab_rows = jnp.take(jnp.stack(shifted), order, axis=0)
    partner = lax.all_gather(piece, ROW, axis=0)
    result = jnp.einsum("pmi,rpki->rmk", slab_rows, partner, preferred_element_type=jnp.float32)
    result = result.astype(jnp.bfloat16)
    row_count = partner.shape[0]
    rows_tile = 128

    def relayout(in_ref, out_ref):
        out_ref[...] = pltpu.einshape("rmk->mrk", in_ref[...])

    result = pl.pallas_call(
        relayout,
        grid=(rows_local // rows_tile,),
        in_specs=[pl.BlockSpec((row_count, rows_tile, share), lambda i: (0, i, 0))],
        out_specs=pl.BlockSpec((rows_tile, row_count, share), lambda i: (i, 0, 0)),
        out_shape=jax.ShapeDtypeStruct((rows_local, row_count, share), jnp.bfloat16),
    )(result)
    return result.reshape(rows_local, row_count, 1, share)


def solution(mesh):
    aux_count, row_count = mesh.devices.shape
    devices = mesh.devices.reshape(aux_count, row_count // 2, 2)
    split_mesh = Mesh(devices, ("aux",) + ROW)
    in_specs = (P("aux", ROW, None), P(ROW, None), P(ROW, None), P(ROW, None))
    out_specs = P(ROW, None, "aux", None)
    return jax.shard_map(
        per_device, mesh=split_mesh, in_specs=in_specs, out_specs=out_specs, check_vma=False
    )
```

```python
import jax
import jax.numpy as jnp
from jax import lax
from jax.experimental import pallas as pl
from jax.experimental.pallas import tpu as pltpu
from jax.sharding import Mesh, PartitionSpec as P


def halo_pieces(block, axis, width):
    count = lax.axis_size(axis)
    forward = [(i, i + 1) for i in range(count - 1)]
    backward = [(target, source) for source, target in forward]
    low = lax.ppermute(lax.slice_in_dim(block, block.shape[0] - width, None, axis=0), axis, forward)
    high = lax.ppermute(lax.slice_in_dim(block, 0, width, axis=0), axis, backward)
    return low, high


ROW = ("rzy", "core")


def per_device(b_tiles, occ_coeff, tile_blocks, screen_mask):
    p_local, rows_local, stored = b_tiles.shape
    blocks_local, slot_count = tile_blocks.shape
    block_size = rows_local // blocks_local
    orbitals = occ_coeff.shape[1]
    aux_count = lax.axis_size("aux")
    row_index = lax.axis_index(ROW)
    low, high = halo_pieces(occ_coeff, ROW, rows_local)
    window = 3 * blocks_local
    local_index = tile_blocks - (row_index - 1) * blocks_local
    local_index = jnp.clip(local_index, 0, window - 1).astype(jnp.int32)
    tiles = b_tiles.reshape(rows_local, stored)

    quarters = 4
    quarter = stored // quarters

    def kernel(index_ref, mask_ref, *refs):
        tile_refs = refs[:quarters]
        low_ref, own_ref, high_ref, out_ref, coeff_ref, rhs_ref = refs[quarters:]
        b = pl.program_id(0)

        @pl.when(b == 0)
        def _():
            coeff_ref[0:rows_local, :] = low_ref[...]
            coeff_ref[rows_local:2 * rows_local, :] = own_ref[...]
            coeff_ref[2 * rows_local:3 * rows_local, :] = high_ref[...]

        for s in range(slot_count):
            start = pl.multiple_of(index_ref[b, s] * block_size, block_size)
            coeff = coeff_ref[pl.ds(start, block_size), :]
            coeff = jnp.where(mask_ref[b, s] != 0, coeff, jnp.zeros_like(coeff))
            rhs_ref[s * block_size:(s + 1) * block_size, :] = coeff
        acc = jnp.zeros(out_ref.shape, jnp.float32)
        for q in range(quarters):
            rhs = rhs_ref[q * quarter:(q + 1) * quarter, :]
            acc = acc + jnp.dot(tile_refs[q][...], rhs, preferred_element_type=jnp.float32)
        out_ref[...] = acc.astype(out_ref.dtype)

    whole = pl.BlockSpec((rows_local, orbitals), lambda b, li, mk: (0, 0))
    half_local = pl.pallas_call(
        kernel,
        grid_spec=pltpu.PrefetchScalarGridSpec(
            num_scalar_prefetch=2,
            grid=(blocks_local,),
            in_specs=[
                pl.BlockSpec((block_size, quarter), lambda b, li, mk, q=q: (b, q))
                for q in range(quarters)
            ]
            + [
                whole,
                whole,
                whole,
            ],
            out_specs=pl.BlockSpec((block_size, orbitals), lambda b, li, mk: (b, 0)),
            scratch_shapes=[
                pltpu.VMEM((window * block_size, orbitals), occ_coeff.dtype),
                pltpu.VMEM((stored, orbitals), occ_coeff.dtype),
            ],
        ),
        out_shape=jax.ShapeDtypeStruct((rows_local, orbitals), jnp.bfloat16),
        compiler_params=pltpu.CompilerParams(dimension_semantics=("arbitrary",)),
    )(local_index, screen_mask, *([tiles] * quarters), low, occ_coeff, high)
    half_local = half_local.reshape(p_local, rows_local, orbitals)
    aux_index = lax.axis_index("aux")
    share = rows_local // aux_count
    own = half_local[0]
    shifted = [own]
    for shift in range(1, aux_count):
        pairs = [(i, (i + shift) % aux_count) for i in range(aux_count)]
        shifted.append(lax.ppermute(own, "aux", pairs))
    piece = lax.all_to_all(
        own.reshape(aux_count, share, orbitals), "aux", 0, 0, tiled=True
    )
    order = (aux_index - jnp.arange(aux_count)) % aux_count
    slab_rows = jnp.take(jnp.stack(shifted), order, axis=0)
    partner = lax.all_gather(piece, ROW, axis=0)
    result = jnp.einsum("pmi,rpki->mrk", slab_rows, partner, preferred_element_type=jnp.float32)
    result = jnp.transpose(result.astype(jnp.bfloat16), (1, 0, 2))
    row_count = partner.shape[0]
    rows_tile = 256

    def relayout(in_ref, out_ref):
        out_ref[...] = pltpu.einshape("rmk->mrk", in_ref[...])

    result = pl.pallas_call(
        relayout,
        grid=(rows_local // rows_tile,),
        in_specs=[pl.BlockSpec((row_count, rows_tile, share), lambda i: (0, i, 0))],
        out_specs=pl.BlockSpec((rows_tile, row_count, share), lambda i: (i, 0, 0)),
        out_shape=jax.ShapeDtypeStruct((rows_local, row_count, share), jnp.bfloat16),
    )(result)
    return result.reshape(rows_local, row_count, 1, share)


def solution(mesh):
    aux_count, row_count = mesh.devices.shape
    devices = mesh.devices.reshape(aux_count, row_count // 2, 2)
    split_mesh = Mesh(devices, ("aux",) + ROW)
    in_specs = (P("aux", ROW, None), P(ROW, None), P(ROW, None), P(ROW, None))
    out_specs = P(ROW, None, "aux", None)
    return jax.shard_map(
        per_device, mesh=split_mesh, in_specs=in_specs, out_specs=out_specs, check_vma=False
    )
```

```python
import jax
import jax.numpy as jnp
from jax import lax
from jax.experimental import pallas as pl
from jax.experimental.pallas import tpu as pltpu
from jax.sharding import Mesh, PartitionSpec as P


def halo_pieces(block, axis, width):
    count = lax.axis_size(axis)
    forward = [(i, i + 1) for i in range(count - 1)]
    backward = [(target, source) for source, target in forward]
    low = lax.ppermute(lax.slice_in_dim(block, block.shape[0] - width, None, axis=0), axis, forward)
    high = lax.ppermute(lax.slice_in_dim(block, 0, width, axis=0), axis, backward)
    return low, high


ROW = ("rzy", "core")


def per_device(b_tiles, occ_coeff, tile_blocks, screen_mask):
    p_local, rows_local, stored = b_tiles.shape
    blocks_local, slot_count = tile_blocks.shape
    block_size = rows_local // blocks_local
    orbitals = occ_coeff.shape[1]
    aux_count = lax.axis_size("aux")
    row_index = lax.axis_index(ROW)
    low, high = halo_pieces(occ_coeff, ROW, rows_local)
    window = 3 * blocks_local
    local_index = tile_blocks - (row_index - 1) * blocks_local
    local_index = jnp.clip(local_index, 0, window - 1).astype(jnp.int32)
    tiles = b_tiles.reshape(rows_local, stored)

    quarters = 4
    pair = 4
    quarter = stored // quarters

    def kernel(index_ref, mask_ref, *refs):
        tile_refs = refs[:quarters]
        low_ref, own_ref, high_ref, out_ref, coeff_ref, rhs_ref = refs[quarters:]
        b = pl.program_id(0)

        @pl.when(b == 0)
        def _():
            coeff_ref[0:rows_local, :] = low_ref[...]
            coeff_ref[rows_local:2 * rows_local, :] = own_ref[...]
            coeff_ref[2 * rows_local:3 * rows_local, :] = high_ref[...]

        for j in range(pair):
            blk = b * pair + j
            for s in range(slot_count):
                start = pl.multiple_of(index_ref[blk, s] * block_size, block_size)
                coeff = coeff_ref[pl.ds(start, block_size), :]
                coeff = jnp.where(mask_ref[blk, s] != 0, coeff, jnp.zeros_like(coeff))
                rhs_ref[j, s * block_size:(s + 1) * block_size, :] = coeff
            acc = jnp.zeros((block_size, orbitals), jnp.float32)
            for q in range(quarters):
                rhs = rhs_ref[j, q * quarter:(q + 1) * quarter, :]
                tile = tile_refs[q][j * block_size:(j + 1) * block_size, :]
                acc = acc + jnp.dot(tile, rhs, preferred_element_type=jnp.float32)
            out_ref[j * block_size:(j + 1) * block_size, :] = acc.astype(out_ref.dtype)

    whole = pl.BlockSpec((rows_local, orbitals), lambda b, li, mk: (0, 0))
    half_local = pl.pallas_call(
        kernel,
        grid_spec=pltpu.PrefetchScalarGridSpec(
            num_scalar_prefetch=2,
            grid=(blocks_local // pair,),
            in_specs=[
                pl.BlockSpec((pair * block_size, quarter), lambda b, li, mk, q=q: (b, q))
                for q in range(quarters)
            ]
            + [
                whole,
                whole,
                whole,
            ],
            out_specs=pl.BlockSpec((pair * block_size, orbitals), lambda b, li, mk: (b, 0)),
            scratch_shapes=[
                pltpu.VMEM((window * block_size, orbitals), occ_coeff.dtype),
                pltpu.VMEM((pair, stored, orbitals), occ_coeff.dtype),
            ],
        ),
        out_shape=jax.ShapeDtypeStruct((rows_local, orbitals), jnp.bfloat16),
        compiler_params=pltpu.CompilerParams(dimension_semantics=("arbitrary",)),
    )(local_index, screen_mask, *([tiles] * quarters), low, occ_coeff, high)
    half_local = half_local.reshape(p_local, rows_local, orbitals)
    aux_index = lax.axis_index("aux")
    share = rows_local // aux_count
    own = half_local[0]
    shifted = [own]
    for shift in range(1, aux_count):
        pairs = [(i, (i + shift) % aux_count) for i in range(aux_count)]
        shifted.append(lax.ppermute(own, "aux", pairs))
    piece = lax.all_to_all(
        own.reshape(aux_count, share, orbitals), "aux", 0, 0, tiled=True
    )
    order = (aux_index - jnp.arange(aux_count)) % aux_count
    slab_rows = jnp.take(jnp.stack(shifted), order, axis=0)
    partner = lax.all_gather(piece, ROW, axis=0)
    result = jnp.einsum("pmi,rpki->mrk", slab_rows, partner, preferred_element_type=jnp.float32)
    result = jnp.transpose(result.astype(jnp.bfloat16), (1, 0, 2))
    row_count = partner.shape[0]
    rows_tile = 512

    def relayout(in_ref, out_ref):
        out_ref[...] = pltpu.einshape("rmk->mrk", in_ref[...])

    result = pl.pallas_call(
        relayout,
        grid=(rows_local // rows_tile, 2),
        in_specs=[pl.BlockSpec((row_count // 2, rows_tile, share), lambda i, h: (h, i, 0))],
        out_specs=pl.BlockSpec((rows_tile, row_count // 2, share), lambda i, h: (i, h, 0)),
        out_shape=jax.ShapeDtypeStruct((rows_local, row_count, share), jnp.bfloat16),
    )(result)
    return result.reshape(rows_local, row_count, 1, share)


def solution(mesh):
    aux_count, row_count = mesh.devices.shape
    devices = mesh.devices.reshape(aux_count, row_count // 2, 2)
    split_mesh = Mesh(devices, ("aux",) + ROW)
    in_specs = (P("aux", ROW, None), P(ROW, None), P(ROW, None), P(ROW, None))
    out_specs = P(ROW, None, "aux", None)
    return jax.shard_map(
        per_device, mesh=split_mesh, in_specs=in_specs, out_specs=out_specs, check_vma=False
    )
```

```python
import jax
import jax.numpy as jnp
from jax import lax
from jax.experimental import pallas as pl
from jax.experimental.pallas import tpu as pltpu
from jax.sharding import Mesh, PartitionSpec as P


def halo_pieces(block, axis, width):
    count = lax.axis_size(axis)
    forward = [(i, i + 1) for i in range(count - 1)]
    backward = [(target, source) for source, target in forward]
    low = lax.ppermute(lax.slice_in_dim(block, block.shape[0] - width, None, axis=0), axis, forward)
    high = lax.ppermute(lax.slice_in_dim(block, 0, width, axis=0), axis, backward)
    return low, high


ROW = ("rzy", "core")


def per_device(b_tiles, occ_coeff, tile_blocks, screen_mask):
    p_local, rows_local, stored = b_tiles.shape
    blocks_local, slot_count = tile_blocks.shape
    block_size = rows_local // blocks_local
    orbitals = occ_coeff.shape[1]
    aux_count = lax.axis_size("aux")
    row_index = lax.axis_index(ROW)
    low, high = halo_pieces(occ_coeff, ROW, rows_local)
    window = 3 * blocks_local
    local_index = tile_blocks - (row_index - 1) * blocks_local
    local_index = jnp.clip(local_index, 0, window - 1).astype(jnp.int32)
    tiles = b_tiles.reshape(rows_local, stored)

    quarters = 4
    pair = 4
    quarter = stored // quarters

    def kernel(index_ref, mask_ref, *refs):
        tile_refs = refs[:quarters]
        low_ref, own_ref, high_ref, out_ref, coeff_ref, rhs_ref, sems = refs[quarters:]
        b = pl.program_id(0)

        @pl.when(b == 0)
        def _():
            copies = [
                pltpu.make_async_copy(src, coeff_ref.at[k * rows_local:(k + 1) * rows_local], sems.at[k])
                for k, src in enumerate((low_ref, own_ref, high_ref))
            ]
            for c in copies:
                c.start()
            for c in copies:
                c.wait()

        for j in range(pair):
            blk = b * pair + j
            for s in range(slot_count):
                start = pl.multiple_of(index_ref[blk, s] * block_size, block_size)
                coeff = coeff_ref[pl.ds(start, block_size), :]
                coeff = jnp.where(mask_ref[blk, s] != 0, coeff, jnp.zeros_like(coeff))
                rhs_ref[j, s * block_size:(s + 1) * block_size, :] = coeff
            acc = jnp.zeros((block_size, orbitals), jnp.float32)
            for q in range(quarters):
                rhs = rhs_ref[j, q * quarter:(q + 1) * quarter, :]
                tile = tile_refs[q][j * block_size:(j + 1) * block_size, :]
                acc = acc + jnp.dot(tile, rhs, preferred_element_type=jnp.float32)
            out_ref[j * block_size:(j + 1) * block_size, :] = acc.astype(out_ref.dtype)

    whole = pl.BlockSpec(memory_space=pl.ANY)
    half_local = pl.pallas_call(
        kernel,
        grid_spec=pltpu.PrefetchScalarGridSpec(
            num_scalar_prefetch=2,
            grid=(blocks_local // pair,),
            in_specs=[
                pl.BlockSpec((pair * block_size, quarter), lambda b, li, mk, q=q: (b, q))
                for q in range(quarters)
            ]
            + [
                whole,
                whole,
                whole,
            ],
            out_specs=pl.BlockSpec((pair * block_size, orbitals), lambda b, li, mk: (b, 0)),
            scratch_shapes=[
                pltpu.VMEM((window * block_size, orbitals), occ_coeff.dtype),
                pltpu.VMEM((pair, stored, orbitals), occ_coeff.dtype),
                pltpu.SemaphoreType.DMA((3,)),
            ],
        ),
        out_shape=jax.ShapeDtypeStruct((rows_local, orbitals), jnp.bfloat16),
        compiler_params=pltpu.CompilerParams(dimension_semantics=("arbitrary",)),
    )(local_index, screen_mask, *([tiles] * quarters), low, occ_coeff, high)
    half_local = half_local.reshape(p_local, rows_local, orbitals)
    aux_index = lax.axis_index("aux")
    share = rows_local // aux_count
    own = half_local[0]
    shifted = [own]
    for shift in range(1, aux_count):
        pairs = [(i, (i + shift) % aux_count) for i in range(aux_count)]
        shifted.append(lax.ppermute(own, "aux", pairs))
    piece = lax.all_to_all(
        own.reshape(aux_count, share, orbitals), "aux", 0, 0, tiled=True
    )
    order = (aux_index - jnp.arange(aux_count)) % aux_count
    slab_rows = jnp.take(jnp.stack(shifted), order, axis=0)
    partner = lax.all_gather(piece, ROW, axis=0)
    result = jnp.einsum("pmi,rpki->mrk", slab_rows, partner, preferred_element_type=jnp.float32)
    result = jnp.transpose(result.astype(jnp.bfloat16), (1, 0, 2))
    row_count = partner.shape[0]
    rows_tile = 512

    def relayout(in_ref, out_ref):
        out_ref[...] = pltpu.einshape("rmk->mrk", in_ref[...])

    result = pl.pallas_call(
        relayout,
        grid=(rows_local // rows_tile,),
        in_specs=[pl.BlockSpec((row_count, rows_tile, share), lambda i: (0, i, 0))],
        out_specs=pl.BlockSpec((rows_tile, row_count, share), lambda i: (i, 0, 0)),
        out_shape=jax.ShapeDtypeStruct((rows_local, row_count, share), jnp.bfloat16),
    )(result)
    return result.reshape(rows_local, row_count, 1, share)


def solution(mesh):
    aux_count, row_count = mesh.devices.shape
    devices = mesh.devices.reshape(aux_count, row_count // 2, 2)
    split_mesh = Mesh(devices, ("aux",) + ROW)
    in_specs = (P("aux", ROW, None), P(ROW, None), P(ROW, None), P(ROW, None))
    out_specs = P(ROW, None, "aux", None)
    return jax.shard_map(
        per_device, mesh=split_mesh, in_specs=in_specs, out_specs=out_specs, check_vma=False
    )
```
